128 devices in a mesh: wa: 16 (over z, y_hi, core), an: 8 (over y_lo, x).
Axes of the slice: x: 4, y: 4 (y_hi: 2, y_lo: 2; y = y_hi * 2 + y_lo), z: 4, core: 2. Of those that a mesh axis runs over, the one named last changes fastest.
Arguments:
- mass_field: float32 [64, 256, 128, 256], P(None, 'wa', 'an'), may hold values from -8 to 8
- factor_one: float32 [256, 64], replicated, may hold values from -0.375 to 0.375
- factor_two: float32 [256, 64], P('wa'), may hold values from -0.375 to 0.375
- factor_four: float32 [64, 16], replicated, may hold values from -0.75 to 0.75
Outputs:
- gram: float32 [128, 128], P('an')
The draws below stay inside these ranges and needn't reach their ends.
All inputs are finite; a program needn't handle non-finite values.
Results may differ from the reference program's by a relative error of at most 0.0001.
Values sent between devices are 32-bit elements; how exact they have to be, the bound alone decides.
No kernel may reach another device: no remote copies, remote signals or barrier semaphores. Data moves between devices by JAX's collectives and lax.ppermute only.
A program may use at most 128 MiB of HBM per device.

```python
import jax
import jax.numpy as jnp
from jax import lax

N4 = 64
R1 = 64
R2 = 64
R4 = 16
N1 = 256
C2 = 16
N2 = 256
N3 = 128


def draw_mass_field(key, part):
    key_noise, key_shared, key_profile = jax.random.split(key, 3)
    shared = jax.random.normal(key_shared, (N4, N2, 1, N1), jnp.float32)
    profile = jax.random.uniform(key_profile, (1, 1, N3, 1), jnp.float32, 0.5, 1.5)
    noise = jax.random.normal(key_noise, (N4, N2, N3, N1), jnp.float32)
    values = noise + shared * profile
    return jnp.clip(values, -8.0, 8.0).astype(jnp.float32)


def level_of(own_key, extent, pieces, smallest, largest):
    gain, own = 1.0, jax.random.fold_in(own_key, 6)
    for dim, parts in pieces:
        draws = jnp.exp(jax.random.uniform(jax.random.fold_in(own, dim), (parts,), jnp.float32, smallest / len(pieces), largest / len(pieces)))
        gain = gain * jnp.repeat(draws, extent[dim] // parts).reshape([-1 if axis == dim else 1 for axis in range(len(extent))])
    return gain


def centred(stream_key, dims, deviation, most, shards=(), dtype=jnp.bfloat16):
    drawn = jax.random.normal(stream_key, dims, jnp.float32) * deviation
    if len(shards) > 0:
        drawn = level_of(stream_key, dims, shards, -0.22, 0.18) * drawn
    return jnp.clip(drawn, min=-most, max=most).astype(dtype)


def setup_inputs(seed: int = 0) -> dict:
    seeds = jax.random.split(jax.random.key(seed), 5)
    mass_field = draw_mass_field(jax.random.fold_in(seeds[4], 71), 0)
    factor_one = centred(seeds[1], (N1, R1), N1 ** -0.5, 0.375, (), jnp.float32)
    factor_two = centred(seeds[2], (N2, R2), N2 ** -0.5, 0.375, ((0, 16),), jnp.float32)
    factor_four = centred(seeds[3], (N4, R4), N4 ** -0.5, 0.75, (), jnp.float32)
    return {"mass_field": mass_field, "factor_one": factor_one, "factor_two": factor_two, "factor_four": factor_four}


def reference(mass_field, factor_one, factor_two, factor_four):
    blocks = N2 // C2
    highest = lax.Precision.HIGHEST

    def add_block(index_block, projected):
        begin = (index_block * C2).astype(jnp.int32)
        piece = lax.dynamic_slice_in_dim(mass_field, begin, C2, 1)
        factor_piece = lax.dynamic_slice_in_dim(factor_two, begin, C2, 0)
        reduced = jnp.dot(factor_four.T, piece.reshape(N4, C2 * N3 * N1), precision=highest)
        mixed_rows = jnp.dot(reduced.reshape(R4 * C2 * N3, N1), factor_one, precision=highest)
        mixed_rows = mixed_rows.reshape(R4, C2, N3, R1)
        contribution = jnp.einsum("qjkr,jp->rkqp", mixed_rows, factor_piece, precision=highest)
        return projected + contribution.reshape(R1, N3, R4 * R2)

    start_value = jnp.zeros((R1, N3, R4 * R2), jnp.float32)
    projected = lax.fori_loop(0, blocks, add_block, start_value)
    summed = jnp.einsum("rim,rjm->ij", projected, projected, precision=highest)
    return summed / (R1 * R2 * R4)
```

```python
import jax
import jax.numpy as jnp
from jax import lax
from jax.sharding import PartitionSpec as P


def on_device(mass_field, factor_one, factor_two, factor_four):
    highest = lax.Precision.HIGHEST
    species_count, fibre_cells, slab_cells, first_cells = mass_field.shape
    rank_one = factor_one.shape[1]
    rank_two = factor_two.shape[1]
    rank_four = factor_four.shape[1]
    fibre_parts = lax.axis_size("wa")
    slab_parts = lax.axis_size("an")
    reduced = jnp.dot(factor_four.T, mass_field.reshape(species_count, -1), precision=highest)
    reduced = reduced.reshape(rank_four * fibre_cells * slab_cells, first_cells)
    mixed_rows = jnp.dot(reduced, factor_one, precision=highest)
    mixed_rows = mixed_rows.reshape(rank_four, fibre_cells, slab_cells, rank_one)
    mixed_rows = lax.all_to_all(mixed_rows, "wa", 3, 1, tiled=True)
    whole_two = lax.all_gather(factor_two, "wa", axis=0, tiled=True)
    projected = jnp.einsum("qjkr,jp->rkqp", mixed_rows, whole_two, precision=highest)
    projected = lax.all_to_all(projected, "an", 2, 1, tiled=True)
    partial_gram = jnp.einsum("rkqp,rlqp->kl", projected, projected, precision=highest)
    gram_rows = lax.psum_scatter(partial_gram, "an", scatter_dimension=0, tiled=True)
    gram_rows = lax.psum(gram_rows, "wa")
    return gram_rows / (rank_one * rank_two * rank_four)


def solution(mesh):
    in_specs = (P(None, "wa", "an", None), P(), P("wa", None), P())
    out_specs = P("an", None)
    return jax.shard_map(
        on_device, mesh=mesh, in_specs=in_specs, out_specs=out_specs, check_vma=False
    )
```

```python
import jax
import jax.numpy as jnp
from jax import lax
from jax.sharding import PartitionSpec as P


def on_device(mass_field, factor_one, factor_two, factor_four):
    highest = lax.Precision.HIGHEST
    species_count, fibre_cells, slab_cells, first_cells = mass_field.shape
    rank_one = factor_one.shape[1]
    rank_two = factor_two.shape[1]
    rank_four = factor_four.shape[1]
    fibre_parts = lax.axis_size("wa")
    slab_parts = lax.axis_size("an")
    devices = fibre_parts * slab_parts
    columns = rank_one * rank_four // devices
    cells = fibre_cells * slab_cells
    reduced = jnp.dot(factor_four.T, mass_field.reshape(species_count, -1), precision=highest)
    reduced = reduced.reshape(rank_four, cells, first_cells)
    mixed = jnp.einsum("ir,qci->rqc", factor_one, reduced, precision=highest)
    mixed = mixed.reshape(devices, columns, cells)
    pieces = fibre_cells * rank_two // cells
    own_two = factor_two.reshape(pieces, 1, cells)
    piece = lax.dynamic_index_in_dim(own_two, lax.axis_index("an") % pieces, 0, keepdims=False)
    payload = jnp.concatenate(
        [mixed, jnp.broadcast_to(piece[None], (devices, 1, cells))], axis=1
    )
    payload = lax.all_to_all(payload, ("wa", "an"), 0, 0, tiled=True)
    payload = payload.reshape(fibre_parts, slab_parts, columns + 1, cells)
    whole_two = payload[:, :pieces, columns, :].reshape(fibre_parts * fibre_cells, rank_two)
    gathered = payload[:, :, :columns, :].reshape(
        fibre_parts, slab_parts, columns, fibre_cells, slab_cells
    )
    whole_two = whole_two.reshape(fibre_parts, fibre_cells, rank_two)
    projected = jnp.einsum("wacjk,wjp->akcp", gathered, whole_two, precision=highest)
    projected = projected.reshape(slab_parts * slab_cells, columns * rank_two)
    partial_gram = jnp.dot(projected, projected.T, precision=highest)
    row_blocks = partial_gram.reshape(1, slab_parts, slab_cells, slab_parts * slab_cells)
    row_blocks = jnp.broadcast_to(
        row_blocks, (fibre_parts, slab_parts, slab_cells, slab_parts * slab_cells)
    ).reshape(devices, slab_cells, slab_parts * slab_cells)
    row_blocks = lax.all_to_all(row_blocks, ("wa", "an"), 0, 0, tiled=True)
    gram_rows = jnp.sum(row_blocks, axis=0)
    return gram_rows / (rank_one * rank_two * rank_four)


def solution(mesh):
    in_specs = (P(None, "wa", "an", None), P(), P("wa", None), P())
    out_specs = P("an", None)
    return jax.shard_map(
        on_device, mesh=mesh, in_specs=in_specs, out_specs=out_specs, check_vma=False
    )
```

```python
import jax
import jax.numpy as jnp
from jax import lax
from jax.sharding import PartitionSpec as P


def on_device(mass_field, factor_one, factor_two, factor_four):
    highest = lax.Precision.HIGHEST
    species_count, fibre_cells, slab_cells, first_cells = mass_field.shape
    rank_one = factor_one.shape[1]
    rank_two = factor_two.shape[1]
    rank_four = factor_four.shape[1]
    fibre_parts = lax.axis_size("wa")
    slab_parts = lax.axis_size("an")
    devices = fibre_parts * slab_parts
    columns = rank_one * rank_four // devices
    halves = rank_four // columns
    spread = jnp.dot(
        mass_field.reshape(species_count * fibre_cells * slab_cells, first_cells),
        factor_one,
        precision=highest,
    ).reshape(species_count, fibre_cells, slab_cells, rank_one)
    mixed = jnp.einsum(
        "shc,sjkr->rhjkc",
        factor_four.reshape(species_count, halves, columns),
        spread,
        precision=highest,
    )
    block = fibre_cells * slab_cells * columns
    mixed = mixed.reshape(devices, block)
    piece_len = fibre_cells * rank_two // slab_parts
    own_two = factor_two.reshape(slab_parts, piece_len)
    piece = lax.dynamic_index_in_dim(own_two, lax.axis_index("an"), 0, keepdims=True)
    payload = jnp.concatenate([mixed, jnp.broadcast_to(piece, (devices, piece_len))], axis=1)
    payload = lax.all_to_all(payload, ("wa", "an"), 0, 0, tiled=True)
    whole_two = payload[:, block:].reshape(fibre_parts, fibre_cells, rank_two)
    gathered = payload[:, :block].reshape(fibre_parts, slab_parts, fibre_cells, slab_cells * columns)
    projected = jnp.einsum("wajx,wjp->axp", gathered, whole_two, precision=highest)
    projected = projected.reshape(slab_parts * slab_cells, columns * rank_two)
    partial_gram = jnp.dot(projected, projected.T, precision=highest)
    row_blocks = partial_gram.reshape(1, slab_parts, slab_cells, slab_parts * slab_cells)
    row_blocks = jnp.broadcast_to(
        row_blocks, (fibre_parts, slab_parts, slab_cells, slab_parts * slab_cells)
    ).reshape(devices, slab_cells, slab_parts * slab_cells)
    row_blocks = lax.all_to_all(row_blocks, ("wa", "an"), 0, 0, tiled=True)
    gram_rows = jnp.sum(row_blocks, axis=0)
    return gram_rows / (rank_one * rank_two * rank_four)


def solution(mesh):
    in_specs = (P(None, "wa", "an", None), P(), P("wa", None), P())
    out_specs = P("an", None)
    return jax.shard_map(
        on_device, mesh=mesh, in_specs=in_specs, out_specs=out_specs, check_vma=False
    )
```

```python
import jax
import jax.numpy as jnp
from jax import lax
from jax.sharding import PartitionSpec as P


def on_device(mass_field, factor_one, factor_two, factor_four):
    highest = lax.Precision.HIGHEST
    species_count, fibre_cells, slab_cells, first_cells = mass_field.shape
    rank_one = factor_one.shape[1]
    rank_two = factor_two.shape[1]
    rank_four = factor_four.shape[1]
    fibre_parts = lax.axis_size("wa")
    slab_parts = lax.axis_size("an")
    devices = fibre_parts * slab_parts
    columns = rank_one * rank_four // devices
    halves = rank_four // columns
    reduced = jnp.einsum(
        "shc,sjki->hjkci",
        factor_four.reshape(species_count, halves, columns),
        mass_field,
        precision=highest,
    )
    mixed = lax.dot_general(
        factor_one,
        reduced.reshape(-1, first_cells),
        (((0,), (1,)), ((), ())),
        precision=highest,
    )
    block = fibre_cells * slab_cells * columns
    mixed = mixed.reshape(devices, block)
    piece_len = fibre_cells * rank_two // slab_parts
    own_two = factor_two.reshape(slab_parts, piece_len)
    piece = lax.dynamic_index_in_dim(own_two, lax.axis_index("an"), 0, keepdims=True)
    payload = jnp.concatenate([mixed, jnp.broadcast_to(piece, (devices, piece_len))], axis=1)
    payload = lax.all_to_all(payload, ("wa", "an"), 0, 0, tiled=True)
    whole_two = payload[:, block:].reshape(fibre_parts, fibre_cells, rank_two)
    gathered = payload[:, :block].reshape(fibre_parts, slab_parts, fibre_cells, slab_cells * columns)
    projected = jnp.einsum("wajx,wjp->axp", gathered, whole_two, precision=highest)
    projected = projected.reshape(slab_parts * slab_cells, columns * rank_two)
    partial_gram = jnp.dot(projected, projected.T, precision=highest)
    row_blocks = partial_gram.reshape(1, slab_parts, slab_cells, slab_parts * slab_cells)
    row_blocks = jnp.broadcast_to(
        row_blocks, (fibre_parts, slab_parts, slab_cells, slab_parts * slab_cells)
    ).reshape(devices, slab_cells, slab_parts * slab_cells)
    row_blocks = lax.all_to_all(row_blocks, ("wa", "an"), 0, 0, tiled=True)
    gram_rows = jnp.sum(row_blocks, axis=0)
    return gram_rows / (rank_one * rank_two * rank_four)


def solution(mesh):
    in_specs = (P(None, "wa", "an", None), P(), P("wa", None), P())
    out_specs = P("an", None)
    return jax.shard_map(
        on_device, mesh=mesh, in_specs=in_specs, out_specs=out_specs, check_vma=False
    )
```

```python
import jax
import jax.numpy as jnp
from jax import lax
from jax.sharding import PartitionSpec as P


def on_device(mass_field, factor_one, factor_two, factor_four):
    highest = lax.Precision.HIGHEST
    species_count, fibre_cells, slab_cells, first_cells = mass_field.shape
    rank_one = factor_one.shape[1]
    rank_two = factor_two.shape[1]
    rank_four = factor_four.shape[1]
    fibre_parts = lax.axis_size("wa")
    slab_parts = lax.axis_size("an")
    devices = fibre_parts * slab_parts
    columns = rank_one * rank_four // devices
    halves = rank_four // columns
    reduced = jnp.einsum(
        "shc,sjki->hjkci",
        factor_four.reshape(species_count, halves, columns),
        mass_field,
        precision=lax.Precision.HIGH,
    )
    mixed = lax.dot_general(
        factor_one,
        reduced.reshape(-1, first_cells),
        (((0,), (1,)), ((), ())),
        precision=highest,
    )
    block = fibre_cells * slab_cells * columns
    mixed = mixed.reshape(devices, block)
    piece_len = fibre_cells * rank_two // slab_parts
    own_two = factor_two.reshape(slab_parts, piece_len)
    piece = lax.dynamic_index_in_dim(own_two, lax.axis_index("an"), 0, keepdims=True)
    payload = jnp.concatenate([mixed, jnp.broadcast_to(piece, (devices, piece_len))], axis=1)
    payload = lax.all_to_all(payload, ("wa", "an"), 0, 0, tiled=True)
    whole_two = payload[:, block:].reshape(fibre_parts, fibre_cells, rank_two)
    gathered = payload[:, :block].reshape(fibre_parts, slab_parts, fibre_cells, slab_cells * columns)
    projected = jnp.einsum("wajx,wjp->axp", gathered, whole_two, precision=highest)
    projected = projected.reshape(slab_parts * slab_cells, columns * rank_two)
    partial_gram = jnp.dot(projected, projected.T, precision=highest)
    row_blocks = partial_gram.reshape(1, slab_parts, slab_cells, slab_parts * slab_cells)
    row_blocks = jnp.broadcast_to(
        row_blocks, (fibre_parts, slab_parts, slab_cells, slab_parts * slab_cells)
    ).reshape(devices, slab_cells, slab_parts * slab_cells)
    row_blocks = lax.all_to_all(row_blocks, ("wa", "an"), 0, 0, tiled=True)
    gram_rows = jnp.sum(row_blocks, axis=0)
    return gram_rows / (rank_one * rank_two * rank_four)


def solution(mesh):
    in_specs = (P(None, "wa", "an", None), P(), P("wa", None), P())
    out_specs = P("an", None)
    return jax.shard_map(
        on_device, mesh=mesh, in_specs=in_specs, out_specs=out_specs, check_vma=False
    )
```

```python
import jax
import jax.numpy as jnp
from jax import lax
from jax.sharding import PartitionSpec as P


def on_device(mass_field, factor_one, factor_two, factor_four):
    highest = lax.Precision.HIGHEST
    species_count, fibre_cells, slab_cells, first_cells = mass_field.shape
    rank_one = factor_one.shape[1]
    rank_two = factor_two.shape[1]
    rank_four = factor_four.shape[1]
    fibre_parts = lax.axis_size("wa")
    slab_parts = lax.axis_size("an")
    devices = fibre_parts * slab_parts
    columns = rank_one * rank_four // devices
    halves = rank_four // columns
    reduced = jnp.einsum(
        "shc,sjki->hjkci",
        factor_four.reshape(species_count, halves, columns),
        mass_field,
        precision=highest,
    )
    mixed = lax.dot_general(
        factor_one,
        reduced.reshape(-1, first_cells),
        (((0,), (1,)), ((), ())),
        precision=highest,
    )
    block = fibre_cells * slab_cells * columns
    mixed = mixed.reshape(devices, block)
    piece_len = fibre_cells * rank_two // slab_parts
    own_two = factor_two.reshape(slab_parts, piece_len)
    piece = lax.dynamic_index_in_dim(own_two, lax.axis_index("an"), 0, keepdims=True)
    payload = jnp.concatenate([mixed, jnp.broadcast_to(piece, (devices, piece_len))], axis=1)
    payload = lax.all_to_all(payload, ("wa", "an"), 0, 0, tiled=True)
    whole_two = payload[:, block:].reshape(fibre_parts, fibre_cells, rank_two)
    gathered = payload[:, :block].reshape(fibre_parts, slab_parts, fibre_cells, slab_cells * columns)
    projected = jnp.einsum("wajx,wjp->axp", gathered, whole_two, precision=highest)
    projected = projected.reshape(slab_parts * slab_cells, columns * rank_two)
    partial_gram = jnp.dot(projected, projected.T, precision=highest)
    row_blocks = partial_gram.reshape(slab_parts, slab_cells, slab_parts * slab_cells)
    row_blocks = lax.all_to_all(row_blocks, "an", 0, 0, tiled=True)
    gram_rows = jnp.sum(row_blocks, axis=0)
    gram_rows = jnp.broadcast_to(gram_rows[None], (fibre_parts,) + gram_rows.shape)
    gram_rows = lax.all_to_all(gram_rows, "wa", 0, 0, tiled=True)
    gram_rows = jnp.sum(gram_rows, axis=0)
    return gram_rows / (rank_one * rank_two * rank_four)


def solution(mesh):
    in_specs = (P(None, "wa", "an", None), P(), P("wa", None), P())
    out_specs = P("an", None)
    return jax.shard_map(
        on_device, mesh=mesh, in_specs=in_specs, out_specs=out_specs, check_vma=False
    )
```

```python
import jax
import jax.numpy as jnp
from jax import lax
from jax.sharding import PartitionSpec as P


def on_device(mass_field, factor_one, factor_two, factor_four):
    highest = lax.Precision.HIGHEST
    species_count, fibre_cells, slab_cells, first_cells = mass_field.shape
    rank_one = factor_one.shape[1]
    rank_two = factor_two.shape[1]
    rank_four = factor_four.shape[1]
    fibre_parts = lax.axis_size("wa")
    slab_parts = lax.axis_size("an")
    devices = fibre_parts * slab_parts
    columns = rank_one * rank_four // devices
    halves = rank_four // columns
    steps = 2
    step_cells = fibre_cells // steps
    block = step_cells * slab_cells * columns
    four = factor_four.reshape(species_count, halves, columns)
    by_fibre = jnp.transpose(mass_field, (1, 2, 0, 3))
    projected = None
    for step in range(steps):
        part = by_fibre[step * step_cells:(step + 1) * step_cells]
        reduced = jnp.einsum("shc,jksi->hjkci", four, part, precision=highest)
        mixed = lax.dot_general(
            factor_one, reduced.reshape(-1, first_cells), (((0,), (1,)), ((), ())), precision=highest
        )
        mixed = mixed.reshape(devices, block)
        piece_len = step_cells * rank_two // slab_parts
        own_two = factor_two[step * step_cells:(step + 1) * step_cells].reshape(slab_parts, piece_len)
        piece = lax.dynamic_index_in_dim(own_two, lax.axis_index("an"), 0, keepdims=True)
        payload = jnp.concatenate([mixed, jnp.broadcast_to(piece, (devices, piece_len))], axis=1)
        payload = lax.all_to_all(payload, ("wa", "an"), 0, 0, tiled=True)
        some_two = payload[:, block:].reshape(fibre_parts, step_cells, rank_two)
        gathered = payload[:, :block].reshape(fibre_parts, slab_parts, step_cells, slab_cells * columns)
        term = jnp.einsum("wajx,wjp->axp", gathered, some_two, precision=highest)
        projected = term if projected is None else projected + term
    projected = projected.reshape(slab_parts * slab_cells, columns * rank_two)
    partial_gram = jnp.dot(projected, projected.T, precision=highest)
    row_blocks = partial_gram.reshape(slab_parts, slab_cells, slab_parts * slab_cells)
    row_blocks = lax.all_to_all(row_blocks, "an", 0, 0, tiled=True)
    gram_rows = jnp.sum(row_blocks, axis=0)
    gram_rows = jnp.broadcast_to(gram_rows[None], (fibre_parts,) + gram_rows.shape)
    gram_rows = lax.all_to_all(gram_rows, "wa", 0, 0, tiled=True)
    gram_rows = jnp.sum(gram_rows, axis=0)
    return gram_rows / (rank_one * rank_two * rank_four)


def solution(mesh):
    in_specs = (P(None, "wa", "an", None), P(), P("wa", None), P())
    out_specs = P("an", None)
    return jax.shard_map(
        on_device, mesh=mesh, in_specs=in_specs, out_specs=out_specs, check_vma=False
    )
```

```python
import jax
import jax.numpy as jnp
from jax import lax
from jax.sharding import PartitionSpec as P


def on_device(mass_field, factor_one, factor_two, factor_four):
    highest = lax.Precision.HIGHEST
    species_count, fibre_cells, slab_cells, first_cells = mass_field.shape
    rank_one = factor_one.shape[1]
    rank_two = factor_two.shape[1]
    rank_four = factor_four.shape[1]
    fibre_parts = lax.axis_size("wa")
    slab_parts = lax.axis_size("an")
    devices = fibre_parts * slab_parts
    columns = rank_one * rank_four // devices
    halves = rank_four // columns
    reduced = jnp.einsum(
        "shc,sjki->hjkci",
        factor_four.reshape(species_count, halves, columns),
        mass_field,
        precision=highest,
    )
    mixed = lax.dot_general(
        factor_one,
        reduced.reshape(-1, first_cells),
        (((0,), (1,)), ((), ())),
        precision=highest,
    )
    block = fibre_cells * slab_cells * columns
    mixed = mixed.reshape(devices, block)
    piece_len = fibre_cells * rank_two // slab_parts
    own_two = factor_two.reshape(slab_parts, piece_len)
    piece = lax.dynamic_index_in_dim(own_two, lax.axis_index("an"), 0, keepdims=True)
    payload = jnp.concatenate([mixed, jnp.broadcast_to(piece, (devices, piece_len))], axis=1)
    payload = lax.all_to_all(payload, ("wa", "an"), 0, 0, tiled=True)
    whole_two = payload[:, block:].reshape(fibre_parts, fibre_cells, rank_two)
    gathered = payload[:, :block].reshape(fibre_parts, slab_parts, fibre_cells, slab_cells * columns)
    projected = jnp.einsum("wajx,wjp->axp", gathered, whole_two, precision=highest)
    projected = projected.reshape(slab_parts * slab_cells, columns * rank_two)
    partial_gram = jnp.dot(projected, projected.T, precision=highest) / (rank_one * rank_two * rank_four)
    row_blocks = partial_gram.reshape(slab_parts, slab_cells, slab_parts * slab_cells)
    row_blocks = lax.all_to_all(row_blocks, "an", 0, 0, tiled=True)
    gram_rows = jnp.sum(row_blocks, axis=0)
    gram_rows = jnp.broadcast_to(gram_rows[None], (fibre_parts,) + gram_rows.shape)
    gram_rows = lax.all_to_all(gram_rows, "wa", 0, 0, tiled=True)
    gram_rows = jnp.sum(gram_rows, axis=0)
    return gram_rows


def solution(mesh):
    in_specs = (P(None, "wa", "an", None), P(), P("wa", None), P())
    out_specs = P("an", None)
    return jax.shard_map(
        on_device, mesh=mesh, in_specs=in_specs, out_specs=out_specs, check_vma=False
    )
```

```python
import jax
import jax.numpy as jnp
from jax import lax
from jax.sharding import PartitionSpec as P


def on_device(mass_field, factor_one, factor_two, factor_four):
    highest = lax.Precision.HIGHEST
    species_count, fibre_cells, slab_cells, first_cells = mass_field.shape
    rank_one = factor_one.shape[1]
    rank_two = factor_two.shape[1]
    rank_four = factor_four.shape[1]
    fibre_parts = lax.axis_size("wa")
    slab_parts = lax.axis_size("an")
    devices = fibre_parts * slab_parts
    columns = rank_one * rank_four // devices
    halves = rank_four // columns
    reduced = jnp.einsum(
        "shc,sjki->hjkci",
        factor_four.reshape(species_count, halves, columns),
        mass_field,
        precision=highest,
    )
    mixed = lax.dot_general(
        factor_one,
        reduced.reshape(-1, first_cells),
        (((0,), (1,)), ((), ())),
        precision=highest,
    )
    block = fibre_cells * slab_cells * columns
    mixed = mixed.reshape(devices, block)
    piece_len = fibre_cells * rank_two // slab_parts
    own_two = factor_two.reshape(slab_parts, piece_len)
    piece = lax.dynamic_index_in_dim(own_two, lax.axis_index("an"), 0, keepdims=True)
    payload = jnp.concatenate([mixed, jnp.broadcast_to(piece, (devices, piece_len))], axis=1)
    payload = lax.all_to_all(payload, ("an", "wa"), 0, 0, tiled=True)
    payload = payload.reshape(slab_parts, fibre_parts, block + piece_len).transpose(1, 0, 2)
    whole_two = payload[:, :, block:].reshape(fibre_parts, fibre_cells, rank_two)
    gathered = payload[:, :, :block].reshape(fibre_parts, slab_parts, fibre_cells, slab_cells * columns)
    projected = jnp.einsum("wajx,wjp->axp", gathered, whole_two, precision=highest)
    projected = projected.reshape(slab_parts * slab_cells, columns * rank_two)
    partial_gram = jnp.dot(projected, projected.T, precision=highest)
    row_blocks = partial_gram.reshape(slab_parts, slab_cells, slab_parts * slab_cells)
    row_blocks = lax.all_to_all(row_blocks, "an", 0, 0, tiled=True)
    gram_rows = jnp.sum(row_blocks, axis=0)
    gram_rows = jnp.broadcast_to(gram_rows[None], (fibre_parts,) + gram_rows.shape)
    gram_rows = lax.all_to_all(gram_rows, "wa", 0, 0, tiled=True)
    gram_rows = jnp.sum(gram_rows, axis=0)
    return gram_rows / (rank_one * rank_two * rank_four)


def solution(mesh):
    in_specs = (P(None, "wa", "an", None), P(), P("wa", None), P())
    out_specs = P("an", None)
    return jax.shard_map(
        on_device, mesh=mesh, in_specs=in_specs, out_specs=out_specs, check_vma=False
    )
```

```python
import jax
import jax.numpy as jnp
from jax import lax
from jax.experimental import pallas as pl
from jax.sharding import PartitionSpec as P


def species_kernel(weights_ref, field_ref, out_ref):
    weights = weights_ref[...]
    rows = weights.shape[1] // field_ref.shape[0]
    for part in range(field_ref.shape[2] // rows):
        block = field_ref[:, 0, part * rows:(part + 1) * rows, :].reshape(weights.shape[1], field_ref.shape[3])
        out = jnp.dot(weights, block, precision=lax.Precision.HIGHEST, preferred_element_type=jnp.float32)
        out_ref[:, 0, part * rows:(part + 1) * rows] = out.reshape(
            out_ref.shape[0], rows, out_ref.shape[3], out_ref.shape[4]
        )


def reduce_species(mass_field, factor_four, columns, rows):
    species_count, fibre_cells, slab_cells, first_cells = mass_field.shape
    rank_four = factor_four.shape[1]
    halves = rank_four // columns
    weights = factor_four.reshape(species_count, halves, 1, columns, 1).transpose(1, 2, 3, 0, 4)
    weights = weights * jnp.eye(rows, dtype=factor_four.dtype).reshape(1, rows, 1, 1, rows)
    weights = weights.reshape(rank_four * rows, species_count * rows)
    return pl.pallas_call(
        species_kernel,
        grid=(fibre_cells,),
        in_specs=[
            pl.BlockSpec((rank_four * rows, species_count * rows), lambda g: (0, 0)),
            pl.BlockSpec((species_count, 1, slab_cells, first_cells), lambda g: (0, g, 0, 0)),
        ],
        out_specs=pl.BlockSpec((halves, 1, slab_cells, columns, first_cells), lambda g: (0, g, 0, 0, 0)),
        out_shape=jax.ShapeDtypeStruct(
            (halves, fibre_cells, slab_cells, columns, first_cells), jnp.float32
        ),
    )(weights, mass_field)


def on_device(mass_field, factor_one, factor_two, factor_four):
    highest = lax.Precision.HIGHEST
    species_count, fibre_cells, slab_cells, first_cells = mass_field.shape
    rank_one = factor_one.shape[1]
    rank_two = factor_two.shape[1]
    rank_four = factor_four.shape[1]
    fibre_parts = lax.axis_size("wa")
    slab_parts = lax.axis_size("an")
    devices = fibre_parts * slab_parts
    columns = rank_one * rank_four // devices
    halves = rank_four // columns
    reduced = reduce_species(mass_field, factor_four, columns, 4)
    mixed = lax.dot_general(
        factor_one,
        reduced.reshape(-1, first_cells),
        (((0,), (1,)), ((), ())),
        precision=highest,
    )
    block = fibre_cells * slab_cells * columns
    mixed = mixed.reshape(devices, block)
    piece_len = fibre_cells * rank_two // slab_parts
    own_two = factor_two.reshape(slab_parts, piece_len)
    piece = lax.dynamic_index_in_dim(own_two, lax.axis_index("an"), 0, keepdims=True)
    payload = jnp.concatenate([mixed, jnp.broadcast_to(piece, (devices, piece_len))], axis=1)
    payload = lax.all_to_all(payload, ("wa", "an"), 0, 0, tiled=True)
    whole_two = payload[:, block:].reshape(fibre_parts, fibre_cells, rank_two)
    gathered = payload[:, :block].reshape(fibre_parts, slab_parts, fibre_cells, slab_cells * columns)
    projected = jnp.einsum("wajx,wjp->axp", gathered, whole_two, precision=highest)
    projected = projected.reshape(slab_parts * slab_cells, columns * rank_two)
    partial_gram = jnp.dot(projected, projected.T, precision=highest)
    row_blocks = partial_gram.reshape(slab_parts, slab_cells, slab_parts * slab_cells)
    row_blocks = lax.all_to_all(row_blocks, "an", 0, 0, tiled=True)
    gram_rows = jnp.sum(row_blocks, axis=0)
    gram_rows = jnp.broadcast_to(gram_rows[None], (fibre_parts,) + gram_rows.shape)
    gram_rows = lax.all_to_all(gram_rows, "wa", 0, 0, tiled=True)
    gram_rows = jnp.sum(gram_rows, axis=0)
    return gram_rows / (rank_one * rank_two * rank_four)


def solution(mesh):
    in_specs = (P(None, "wa", "an", None), P(), P("wa", None), P())
    out_specs = P("an", None)
    return jax.shard_map(
        on_device, mesh=mesh, in_specs=in_specs, out_specs=out_specs, check_vma=False
    )
```

```python
import jax
import jax.numpy as jnp
from jax import lax
from jax.sharding import PartitionSpec as P


def on_device(mass_field, factor_one, factor_two, factor_four):
    highest = lax.Precision.HIGHEST
    species_count, fibre_cells, slab_cells, first_cells = mass_field.shape
    rank_one = factor_one.shape[1]
    rank_two = factor_two.shape[1]
    rank_four = factor_four.shape[1]
    fibre_parts = lax.axis_size("wa")
    slab_parts = lax.axis_size("an")
    devices = fibre_parts * slab_parts
    columns = rank_one * rank_four // devices
    halves = rank_four // columns
    reduced = jnp.einsum(
        "shc,sjki->hjkci",
        factor_four.reshape(species_count, halves, columns),
        mass_field,
        precision=highest,
    )
    mixed = lax.dot_general(
        factor_one,
        reduced.reshape(-1, first_cells),
        (((0,), (1,)), ((), ())),
        precision=highest,
    )
    block = fibre_cells * slab_cells * columns
    mixed = mixed.reshape(devices, block)
    piece_len = fibre_cells * rank_two // slab_parts
    own_two = factor_two.reshape(slab_parts, piece_len)
    piece = lax.dynamic_index_in_dim(own_two, lax.axis_index("an"), 0, keepdims=True)
    payload = jnp.concatenate([mixed, jnp.broadcast_to(piece, (devices, piece_len))], axis=1)
    payload = lax.all_to_all(payload, ("wa", "an"), 0, 0, tiled=True)
    whole_two = payload[:, block:].reshape(fibre_parts, fibre_cells, rank_two)
    gathered = payload[:, :block].reshape(fibre_parts, slab_parts, fibre_cells, slab_cells * columns)
    projected = jnp.einsum("wajx,wjp->axp", gathered, whole_two, precision=highest)
    projected = projected.reshape(slab_parts * slab_cells, columns * rank_two)
    partial_gram = jnp.dot(projected, projected.T, precision=highest)
    row_blocks = partial_gram.reshape(slab_parts, slab_cells, slab_parts * slab_cells)
    row_blocks = lax.all_to_all(row_blocks, "an", 0, 0, tiled=True)
    gram_rows = jnp.sum(row_blocks, axis=0)
    gram_rows = gram_rows + lax.ppermute(gram_rows, "wa", [(i, i ^ 1) for i in range(fibre_parts)])
    groups = [list(range(core, fibre_parts, 2)) for core in range(2)]
    gram_rows = jnp.broadcast_to(gram_rows[None], (fibre_parts // 2,) + gram_rows.shape)
    gram_rows = lax.all_to_all(gram_rows, "wa", 0, 0, axis_index_groups=groups, tiled=True)
    gram_rows = jnp.sum(gram_rows, axis=0)
    return gram_rows / (rank_one * rank_two * rank_four)


def solution(mesh):
    in_specs = (P(None, "wa", "an", None), P(), P("wa", None), P())
    out_specs = P("an", None)
    return jax.shard_map(
        on_device, mesh=mesh, in_specs=in_specs, out_specs=out_specs, check_vma=False
    )
```

```python
import jax
import jax.numpy as jnp
from jax import lax
from jax.sharding import PartitionSpec as P


def on_device(mass_field, factor_one, factor_two, factor_four):
    highest = lax.Precision.HIGHEST
    species_count, fibre_cells, slab_cells, first_cells = mass_field.shape
    rank_one = factor_one.shape[1]
    rank_two = factor_two.shape[1]
    rank_four = factor_four.shape[1]
    fibre_parts = lax.axis_size("wa")
    slab_parts = lax.axis_size("an")
    devices = fibre_parts * slab_parts
    columns = rank_one * rank_four // devices
    halves = rank_four // columns
    reduced = jnp.einsum(
        "shc,sjki->hjkci",
        factor_four.reshape(species_count, halves, columns),
        mass_field,
        precision=highest,
    )
    mixed = lax.dot_general(
        factor_one,
        reduced.reshape(-1, first_cells),
        (((0,), (1,)), ((), ())),
        precision=highest,
    )
    block = fibre_cells * slab_cells * columns
    mixed = mixed.reshape(devices, block)
    piece_len = fibre_cells * rank_two // slab_parts
    own_two = factor_two.reshape(slab_parts, piece_len)
    piece = lax.dynamic_index_in_dim(own_two, lax.axis_index("an"), 0, keepdims=True)
    payload = jnp.concatenate(
        [mixed[:, None, :], jnp.broadcast_to(piece[None], (devices, 1, piece_len))], axis=2
    )
    payload = lax.all_to_all(payload, ("wa", "an"), 0, 0, tiled=True).reshape(devices, -1)
    whole_two = payload[:, block:].reshape(fibre_parts, fibre_cells, rank_two)
    gathered = payload[:, :block].reshape(fibre_parts, slab_parts, fibre_cells, slab_cells * columns)
    projected = jnp.einsum("wajx,wjp->axp", gathered, whole_two, precision=highest)
    projected = projected.reshape(slab_parts * slab_cells, columns * rank_two)
    partial_gram = jnp.dot(projected, projected.T, precision=highest)
    row_blocks = partial_gram.reshape(slab_parts, slab_cells, slab_parts * slab_cells)
    row_blocks = lax.all_to_all(row_blocks, "an", 0, 0, tiled=True)
    gram_rows = jnp.sum(row_blocks, axis=0)
    gram_rows = jnp.broadcast_to(gram_rows[None], (fibre_parts,) + gram_rows.shape)
    gram_rows = lax.all_to_all(gram_rows, "wa", 0, 0, tiled=True)
    gram_rows = jnp.sum(gram_rows, axis=0)
    return gram_rows / (rank_one * rank_two * rank_four)


def solution(mesh):
    in_specs = (P(None, "wa", "an", None), P(), P("wa", None), P())
    out_specs = P("an", None)
    return jax.shard_map(
        on_device, mesh=mesh, in_specs=in_specs, out_specs=out_specs, check_vma=False
    )
```
